512 devices in a mesh: dom: 32 (over x, z), strip: 16 (over y, core).
Axes of the slice: x: 4, y: 8, z: 8, core: 2. Of those that a mesh axis runs over, the one named last changes fastest.
Arguments:
- state: float32 [32, 4, 512, 512], P('dom', None, 'strip'), may hold values from -6 to 6
- copies: int32 [32], replicated, may hold values from 0 to 31
- depth: float32 [512, 512], P('strip'), may hold values from 0.5 to 2
- friction: float32 [512, 512], P('strip'), may hold values from 0.05 to 0.5
- obs_cells: int32 [16, 512], P('strip'), may hold values from 0 to 16383
- obs_values: float32 [16, 512], P('strip'), may hold values from -6 to 6
Outputs:
- forecast: float32 [32, 4, 512, 512], P('dom', None, 'strip')
- log_weights: float32 [32], P('dom')
The draws below stay inside these ranges and needn't reach their ends.
All inputs are finite; a program needn't handle non-finite values.
Results may differ from the reference program's by a relative error of at most 0.000039.
Values sent between devices are 32-bit elements; how exact they have to be, the bound alone decides.
No kernel may reach another device: no remote copies, remote signals or barrier semaphores. Data moves between devices by JAX's collectives and lax.ppermute only.
A program may use at most 64 MiB of HBM per device.

```python
import math
import jax
import jax.numpy as jnp

ROWS_DEV = 32
COLS = 512
OBS_DEV = 512
STEPS = 4
PARTICLES = 32
NY = 512
N_STRIP = 16


def draw_copies(key, part):
    count = PARTICLES
    keys = jax.random.split(jax.random.fold_in(key, 17), 5)
    slot = jnp.arange(count, dtype=jnp.int32)
    popular = jax.random.randint(keys[0], (3,), 0, count, dtype=jnp.int32)
    which = jax.random.randint(keys[1], (count,), 0, 3, dtype=jnp.int32)
    from_popular = jnp.where(which == 0, popular[0], jnp.where(which == 1, popular[1], popular[2]))
    offset = jax.random.randint(keys[2], (count,), 0, count, dtype=jnp.int32)
    shifted = (slot + offset) % count
    usage = jax.random.randint(keys[3], (count,), 0, 2, dtype=jnp.int32)
    result = jnp.where(usage == 1, from_popular, shifted)
    anchor = jax.random.randint(keys[4], (), 0, count, dtype=jnp.int32)
    result = jnp.where(slot == anchor, (anchor + count // 2) % count, result)
    result = jnp.where(slot == (anchor + 1) % count, (anchor + 2) % count, result)
    result = jnp.where(slot == (anchor + 2) % count, (anchor + 1) % count, result)
    result = jnp.where(slot == (anchor + 3) % count, count - 1, result)
    result = jnp.where(slot == (anchor + 4) % count, 0, result)
    return result.astype(jnp.int32)


def touch_ends(drawn, stream_key, smallest, high):
    spot = [jax.random.randint(jax.random.fold_in(stream_key, axis), (), 0, length) for axis, length in enumerate(drawn.shape)]
    longest = drawn.shape.index(max(drawn.shape))
    neighbour = spot[:longest] + [(spot[longest] + 1) % drawn.shape[longest]] + spot[longest + 1:]
    return drawn.at[tuple(spot)].set(smallest).at[tuple(neighbour)].set(high)


def level_of(key, extent, shards, low, high):
    loudness, own = 1.0, jax.random.fold_in(key, 6)
    for position, shards_of in shards:
        heights = jnp.exp(jax.random.uniform(jax.random.fold_in(own, position), (shards_of,), jnp.float32, low / len(shards), high / len(shards)))
        loudness = loudness * jnp.repeat(heights, extent[position] // shards_of).reshape([-1 if axis == position else 1 for axis in range(len(extent))])
    return loudness


def gaussian(key, dims, width, most, cuts=(), kind=jnp.bfloat16):
    factor_of = level_of(key, dims, cuts, -0.22, 0.18) if cuts else 1.0
    values = jax.random.normal(key, dims, jnp.float32) * width * factor_of
    return jnp.minimum(jnp.maximum(values, -most), most).astype(kind)


def setup_inputs(seed: int = 0) -> dict:
    streams_of = jax.random.split(jax.random.key(seed), 7)
    state = gaussian(streams_of[0], (PARTICLES, 4, NY, COLS), 1.0, 6.0, ((0, 32), (2, 16)), jnp.float32)
    copies = draw_copies(jax.random.fold_in(streams_of[6], 71), 0)
    depth = jnp.clip(jnp.exp(math.log(2.0) - 1.3862944 * jax.random.uniform(streams_of[2], (NY, COLS), jnp.float32) ** level_of(streams_of[2], (NY, COLS), ((0, 16),), -0.2, 0.2)), 0.5, 2.0)
    friction = jnp.clip(jnp.exp(math.log(0.5) - 2.3025851 * jax.random.uniform(streams_of[3], (NY, COLS), jnp.float32) ** level_of(streams_of[3], (NY, COLS), ((0, 16),), -0.2, 0.2)), 0.05, 0.5)
    obs_cells = touch_ends(jax.random.randint(streams_of[4], (N_STRIP, OBS_DEV), 0, ROWS_DEV * COLS), jax.random.fold_in(streams_of[4], 1), 0, (ROWS_DEV * COLS) - 1).astype(jnp.int32)
    obs_values = gaussian(streams_of[5], (N_STRIP, OBS_DEV), 1.0, 6.0, ((0, 16),), jnp.float32)
    return {"state": state, "copies": copies, "depth": depth, "friction": friction, "obs_cells": obs_cells, "obs_values": obs_values}


time_step = 0.25
coriolis = 0.3
diffusion = 0.2
obs_variance = 4.0


def diff_cols(a):
    return (jnp.roll(a, -1, axis=-1) - jnp.roll(a, 1, axis=-1)) * 0.5


def pad_rows(a):
    return jnp.pad(a, ((0, 0), (1, 1), (0, 0)))


def advance(member, depth, friction):
    eta, velo_u, velo_v, tracer = member[:, 0], member[:, 1], member[:, 2], member[:, 3]
    flux_x = depth * velo_u
    flux_y = pad_rows(depth * velo_v)
    eta_new = eta - time_step * (diff_cols(flux_x) + (flux_y[:, 2:] - flux_y[:, :-2]) * 0.5)
    eta_pad = pad_rows(eta_new)
    u_new = velo_u - time_step * diff_cols(eta_new) - time_step * friction * velo_u + time_step * coriolis * velo_v
    v_new = velo_v - time_step * ((eta_pad[:, 2:] - eta_pad[:, :-2]) * 0.5) - time_step * friction * velo_v - time_step * coriolis * velo_u
    tracer_pad = pad_rows(tracer)
    upper = tracer_pad[:, 2:]
    lower = tracer_pad[:, :-2]
    grad_y = (upper - lower) * 0.5
    laplace = upper + lower + jnp.roll(tracer, -1, axis=-1) + jnp.roll(tracer, 1, axis=-1) - 4.0 * tracer
    c_new = tracer - time_step * (velo_u * diff_cols(tracer) + velo_v * grad_y) + time_step * diffusion * laplace
    return jnp.stack([eta_new, u_new, v_new, c_new], axis=1)


def reference(state, copies, depth, friction, obs_cells, obs_values):
    member = jnp.take(state, copies, axis=0)
    for step in range(STEPS):
        member = advance(member, depth, friction)
    eta = member[:, 0].reshape(member.shape[0], -1)
    offsets = (jnp.arange(obs_cells.shape[0], dtype=jnp.int32) * (ROWS_DEV * COLS)).astype(jnp.int32)
    flat_index = (obs_cells + offsets[:, None]).reshape(-1).astype(jnp.int32)
    seen = jnp.take(eta, flat_index, axis=1)
    gap = seen - obs_values.reshape(-1)[None, :]
    loglik = -jnp.sum(gap * gap, axis=1) * (0.5 / obs_variance)
    top = jnp.max(loglik)
    total = top + jnp.log(jnp.sum(jnp.exp(loglik - top)))
    return member, loglik - total
```

```python
import jax
import jax.numpy as jnp
from jax import lax
from jax.sharding import Mesh
from jax.sharding import PartitionSpec as P

STEPS = 4


time_step = 0.25
coriolis = 0.3
diffusion = 0.2
obs_variance = 4.0

DOM = ("dx", "dz")


def diff_cols(a):
    return (jnp.roll(a, -1, axis=-1) - jnp.roll(a, 1, axis=-1)) * 0.5


def advance(padded, deep, drag, valid):
    eta, velo_u, velo_v, tracer = (padded[:, 0], padded[:, 1], padded[:, 2], padded[:, 3])
    flux_x = deep * velo_u
    flux_y = deep * velo_v
    eta_ext = eta[:, 1:-1] - time_step * (
        diff_cols(flux_x)[:, 1:-1] + (flux_y[:, 2:] - flux_y[:, :-2]) * 0.5
    )
    eta_ext = jnp.where(valid, eta_ext, 0.0)
    eta_new = eta_ext[:, 1:-1]
    inner_u = velo_u[:, 2:-2]
    inner_v = velo_v[:, 2:-2]
    inner_r = drag[2:-2]
    u_new = (
        inner_u
        - time_step * diff_cols(eta_new)
        - time_step * inner_r * inner_u
        + time_step * coriolis * inner_v
    )
    v_new = (
        inner_v
        - time_step * ((eta_ext[:, 2:] - eta_ext[:, :-2]) * 0.5)
        - time_step * inner_r * inner_v
        - time_step * coriolis * inner_u
    )
    inner_c = tracer[:, 2:-2]
    upper = tracer[:, 3:-1]
    lower = tracer[:, 1:-3]
    grad_y = (upper - lower) * 0.5
    laplace = (
        upper
        + lower
        + jnp.roll(inner_c, -1, axis=-1)
        + jnp.roll(inner_c, 1, axis=-1)
        - 4.0 * inner_c
    )
    c_new = (
        inner_c
        - time_step * (inner_u * diff_cols(inner_c) + inner_v * grad_y)
        + time_step * diffusion * laplace
    )
    return jnp.stack([eta_new, u_new, v_new, c_new], axis=1)


def halo_frame(cells, width):
    count = lax.axis_size("strip")
    ends = count - 1
    rows = cells.shape[1]
    head = cells[:, :width]
    tail = cells[:, rows - width:]
    above = lax.ppermute(tail, "strip", [(i, i + 1) for i in range(ends)])
    below = lax.ppermute(head, "strip", [(i + 1, i) for i in range(ends)])
    return jnp.concatenate([above, cells, below], axis=1)


def forecast_of(state, depth, friction):
    rows = state.shape[2]
    margin = 2 * STEPS
    packed = jnp.concatenate([state[0], depth[None], friction[None]], axis=0)
    frame = halo_frame(packed, margin)
    member = frame[None, :4]
    deep_all = frame[4]
    drag_all = frame[5]
    strip_idx = lax.axis_index("strip")
    total_rows = rows * lax.axis_size("strip")
    row_all = strip_idx * rows - margin + jnp.arange(rows + 2 * margin, dtype=jnp.int32)
    inside_all = ((row_all >= 0) & (row_all < total_rows))[:, None]
    span = rows + 2 * margin
    for step in range(STEPS):
        lo = 2 * step
        hi = span - 2 * step
        deep = deep_all[lo:hi]
        drag = drag_all[lo:hi]
        valid = inside_all[lo + 1 : hi - 1]
        kept = inside_all[lo + 2 : hi - 2]
        result = advance(member, deep, drag, valid)
        member = jnp.where(kept[None, None], result, 0.0)
    return member


def local(state, copies, depth, friction, obs_cells, obs_values):
    nx = lax.axis_size("dx")
    nz = lax.axis_size("dz")
    n_dom = nx * nz
    mx = lax.axis_index("dx")
    mz = lax.axis_index("dz")
    me = mx * nz + mz

    fore = forecast_of(state, depth, friction)

    eta = fore[0, 0].reshape(-1)
    seen = jnp.take(eta, obs_cells[0], axis=0)
    gap = seen - obs_values[0]
    partial_value = -jnp.sum(gap * gap) * (0.5 / obs_variance)
    slots = jnp.where(jnp.arange(n_dom) == me, partial_value, 0.0)
    by_source = lax.psum(slots, ("dx", "dz", "strip"))

    along_z = lax.all_gather(fore[0], "dz", axis=0, tiled=False)
    dest = jnp.arange(nx) * nz + mz
    src = copies[dest]
    picks = jnp.take(along_z, src % nz, axis=0)
    moved = lax.all_to_all(picks, "dx", 0, 0, tiled=False)
    mine_src = copies[me]
    member = lax.dynamic_index_in_dim(moved, mine_src // nz, axis=0, keepdims=True)

    loglik = by_source[copies]
    top = jnp.max(loglik)
    total = top + jnp.log(jnp.sum(jnp.exp(loglik - top)))
    mine = lax.dynamic_slice_in_dim(loglik - total, me, 1, 0)
    return (member, mine)


def solution(mesh):
    n_dom = mesh.shape["dom"]
    xs = sorted({d.coords[0] for d in mesh.devices[:, 0]})
    nx = len(xs)
    devices = mesh.devices.reshape(nx, n_dom // nx, mesh.shape["strip"])
    split = Mesh(devices, ("dx", "dz", "strip"))
    placed = (
        P(DOM, None, "strip", None),
        P(),
        P("strip", None),
        P("strip", None),
        P("strip", None),
        P("strip", None),
    )
    return jax.shard_map(
        local,
        mesh=split,
        in_specs=placed,
        out_specs=(P(DOM, None, "strip", None), P(DOM)),
        check_vma=False,
    )
```

```python
import jax
import jax.numpy as jnp
from jax import lax
from jax.sharding import Mesh
from jax.sharding import PartitionSpec as P

STEPS = 4


time_step = 0.25
coriolis = 0.3
diffusion = 0.2
obs_variance = 4.0

DOM = ("dx", "dz")
LOGLIK_MODE = "a2a"
STAGE1 = "gather"
STAGE2 = "a2a"


def diff_cols(a):
    return (jnp.roll(a, -1, axis=-1) - jnp.roll(a, 1, axis=-1)) * 0.5


def advance(padded, deep, drag, valid):
    eta, velo_u, velo_v, tracer = (padded[:, 0], padded[:, 1], padded[:, 2], padded[:, 3])
    flux_x = deep * velo_u
    flux_y = deep * velo_v
    eta_ext = eta[:, 1:-1] - time_step * (
        diff_cols(flux_x)[:, 1:-1] + (flux_y[:, 2:] - flux_y[:, :-2]) * 0.5
    )
    eta_ext = jnp.where(valid, eta_ext, 0.0)
    eta_new = eta_ext[:, 1:-1]
    inner_u = velo_u[:, 2:-2]
    inner_v = velo_v[:, 2:-2]
    inner_r = drag[2:-2]
    u_new = (
        inner_u
        - time_step * diff_cols(eta_new)
        - time_step * inner_r * inner_u
        + time_step * coriolis * inner_v
    )
    v_new = (
        inner_v
        - time_step * ((eta_ext[:, 2:] - eta_ext[:, :-2]) * 0.5)
        - time_step * inner_r * inner_v
        - time_step * coriolis * inner_u
    )
    inner_c = tracer[:, 2:-2]
    upper = tracer[:, 3:-1]
    lower = tracer[:, 1:-3]
    grad_y = (upper - lower) * 0.5
    laplace = (
        upper
        + lower
        + jnp.roll(inner_c, -1, axis=-1)
        + jnp.roll(inner_c, 1, axis=-1)
        - 4.0 * inner_c
    )
    c_new = (
        inner_c
        - time_step * (inner_u * diff_cols(inner_c) + inner_v * grad_y)
        + time_step * diffusion * laplace
    )
    return jnp.stack([eta_new, u_new, v_new, c_new], axis=1)


def halo_frame(cells, width):
    count = lax.axis_size("strip")
    ends = count - 1
    rows = cells.shape[1]
    head = cells[:, :width]
    tail = cells[:, rows - width:]
    above = lax.ppermute(tail, "strip", [(i, i + 1) for i in range(ends)])
    below = lax.ppermute(head, "strip", [(i + 1, i) for i in range(ends)])
    return jnp.concatenate([above, cells, below], axis=1)


def forecast_of(state, depth, friction):
    rows = state.shape[2]
    margin = 2 * STEPS
    packed = jnp.concatenate([state[0], depth[None], friction[None]], axis=0)
    frame = halo_frame(packed, margin)
    member = frame[None, :4]
    deep_all = frame[4]
    drag_all = frame[5]
    strip_idx = lax.axis_index("strip")
    total_rows = rows * lax.axis_size("strip")
    row_all = strip_idx * rows - margin + jnp.arange(rows + 2 * margin, dtype=jnp.int32)
    inside_all = ((row_all >= 0) & (row_all < total_rows))[:, None]
    span = rows + 2 * margin
    for step in range(STEPS):
        lo = 2 * step
        hi = span - 2 * step
        deep = deep_all[lo:hi]
        drag = drag_all[lo:hi]
        valid = inside_all[lo + 1 : hi - 1]
        kept = inside_all[lo + 2 : hi - 2]
        result = advance(member, deep, drag, valid)
        member = jnp.where(kept[None, None], result, 0.0)
    return member


def butterfly_sum(value, axes):
    for axis, size in axes:
        step = 1
        while step < size:
            pairs = [(i, i ^ step) for i in range(size)]
            value = value + lax.ppermute(value, axis, pairs)
            step *= 2
    return value


def local(state, copies, depth, friction, obs_cells, obs_values):
    nx = lax.axis_size("dx")
    nz = lax.axis_size("dz")
    n_dom = nx * nz
    mx = lax.axis_index("dx")
    mz = lax.axis_index("dz")
    me = mx * nz + mz

    fore = forecast_of(state, depth, friction)

    eta = fore[0, 0].reshape(-1)
    seen = jnp.take(eta, obs_cells[0], axis=0)
    gap = seen - obs_values[0]
    partial_value = -jnp.sum(gap * gap) * (0.5 / obs_variance)
    if LOGLIK_MODE == "psum":
        slots = jnp.where(jnp.arange(n_dom) == me, partial_value, 0.0)
        by_source = lax.psum(slots, ("dx", "dz", "strip"))
    elif LOGLIK_MODE == "a2a":
        n_all = n_dom * lax.axis_size("strip")
        spread = jnp.broadcast_to(partial_value, (n_all, 1))
        every = lax.all_to_all(spread, ("dx", "dz", "strip"), 0, 0, tiled=True)
        by_source = jnp.sum(every.reshape(n_dom, -1), axis=1)
    else:
        slots = jnp.where(jnp.arange(n_dom) == me, partial_value, 0.0)
        by_source = butterfly_sum(slots, (("strip", lax.axis_size("strip")), ("dx", nx), ("dz", nz)))

    if STAGE1 == "gather":
        along_z = lax.all_gather(fore[0], "dz", axis=0, tiled=False)
    else:
        parts = [None] * nz
        parts[0] = fore[0]
        for d in range(1, nz):
            parts[d] = lax.ppermute(fore[0], "dz", [(i, (i + d) % nz) for i in range(nz)])
        order = jnp.stack(parts)
        along_z = jnp.take(order, (mz - jnp.arange(nz)) % nz, axis=0)
    dest = jnp.arange(nx) * nz + mz
    src = copies[dest]
    picks = jnp.take(along_z, src % nz, axis=0)
    if STAGE2 == "a2a":
        moved = lax.all_to_all(picks, "dx", 0, 0, tiled=False)
    else:
        got = [None] * nx
        got[0] = lax.dynamic_index_in_dim(picks, mx, axis=0, keepdims=False)
        for d in range(1, nx):
            send = lax.dynamic_index_in_dim(picks, (mx + d) % nx, axis=0, keepdims=False)
            got[d] = lax.ppermute(send, "dx", [(i, (i + d) % nx) for i in range(nx)])
        moved = jnp.take(jnp.stack(got), (mx - jnp.arange(nx)) % nx, axis=0)
    mine_src = copies[me]
    member = lax.dynamic_index_in_dim(moved, mine_src // nz, axis=0, keepdims=True)

    loglik = by_source[copies]
    top = jnp.max(loglik)
    total = top + jnp.log(jnp.sum(jnp.exp(loglik - top)))
    mine = lax.dynamic_slice_in_dim(loglik - total, me, 1, 0)
    return (member, mine)


def solution(mesh):
    n_dom = mesh.shape["dom"]
    xs = sorted({d.coords[0] for d in mesh.devices[:, 0]})
    nx = len(xs)
    devices = mesh.devices.reshape(nx, n_dom // nx, mesh.shape["strip"])
    split = Mesh(devices, ("dx", "dz", "strip"))
    placed = (
        P(DOM, None, "strip", None),
        P(),
        P("strip", None),
        P("strip", None),
        P("strip", None),
        P("strip", None),
    )
    return jax.shard_map(
        local,
        mesh=split,
        in_specs=placed,
        out_specs=(P(DOM, None, "strip", None), P(DOM)),
        check_vma=False,
    )
```

```python
import jax
import jax.numpy as jnp
from jax import lax
from jax.sharding import Mesh
from jax.sharding import PartitionSpec as P

STEPS = 4


time_step = 0.25
coriolis = 0.3
diffusion = 0.2
obs_variance = 4.0

DOM = ("dx", "dz")
LOGLIK_MODE = "a2a"
STAGE1 = "gather"
STAGE2 = "a2a"


def diff_cols(a):
    return (jnp.roll(a, -1, axis=-1) - jnp.roll(a, 1, axis=-1)) * 0.5


def advance(padded, deep, drag, valid):
    eta, velo_u, velo_v, tracer = (padded[:, 0], padded[:, 1], padded[:, 2], padded[:, 3])
    flux_x = deep * velo_u
    flux_y = deep * velo_v
    eta_ext = eta[:, 1:-1] - time_step * (
        diff_cols(flux_x)[:, 1:-1] + (flux_y[:, 2:] - flux_y[:, :-2]) * 0.5
    )
    eta_ext = jnp.where(valid, eta_ext, 0.0)
    eta_new = eta_ext[:, 1:-1]
    inner_u = velo_u[:, 2:-2]
    inner_v = velo_v[:, 2:-2]
    inner_r = drag[2:-2]
    u_new = (
        inner_u
        - time_step * diff_cols(eta_new)
        - time_step * inner_r * inner_u
        + time_step * coriolis * inner_v
    )
    v_new = (
        inner_v
        - time_step * ((eta_ext[:, 2:] - eta_ext[:, :-2]) * 0.5)
        - time_step * inner_r * inner_v
        - time_step * coriolis * inner_u
    )
    inner_c = tracer[:, 2:-2]
    upper = tracer[:, 3:-1]
    lower = tracer[:, 1:-3]
    grad_y = (upper - lower) * 0.5
    laplace = (
        upper
        + lower
        + jnp.roll(inner_c, -1, axis=-1)
        + jnp.roll(inner_c, 1, axis=-1)
        - 4.0 * inner_c
    )
    c_new = (
        inner_c
        - time_step * (inner_u * diff_cols(inner_c) + inner_v * grad_y)
        + time_step * diffusion * laplace
    )
    return jnp.stack([eta_new, u_new, v_new, c_new], axis=1)


def halo_frame(cells, width):
    count = lax.axis_size("strip")
    ends = count - 1
    rows = cells.shape[1]
    head = cells[:, :width]
    tail = cells[:, rows - width:]
    above = lax.ppermute(tail, "strip", [(i, i + 1) for i in range(ends)])
    below = lax.ppermute(head, "strip", [(i + 1, i) for i in range(ends)])
    return jnp.concatenate([above, cells, below], axis=1)


def forecast_of(state, depth, friction):
    rows = state.shape[2]
    margin = 2 * STEPS
    packed = jnp.concatenate([state[0], depth[None], friction[None]], axis=0)
    frame = halo_frame(packed, margin)
    member = frame[None, :4]
    deep_all = frame[4]
    drag_all = frame[5]
    strip_idx = lax.axis_index("strip")
    total_rows = rows * lax.axis_size("strip")
    row_all = strip_idx * rows - margin + jnp.arange(rows + 2 * margin, dtype=jnp.int32)
    inside_all = ((row_all >= 0) & (row_all < total_rows))[:, None]
    span = rows + 2 * margin
    for step in range(STEPS):
        lo = 2 * step
        hi = span - 2 * step
        deep = deep_all[lo:hi]
        drag = drag_all[lo:hi]
        valid = inside_all[lo + 1 : hi - 1]
        kept = inside_all[lo + 2 : hi - 2]
        result = advance(member, deep, drag, valid)
        member = jnp.where(kept[None, None], result, 0.0)
    return member


def butterfly_sum(value, axes):
    for axis, size in axes:
        step = 1
        while step < size:
            pairs = [(i, i ^ step) for i in range(size)]
            value = value + lax.ppermute(value, axis, pairs)
            step *= 2
    return value


def local(state, copies, depth, friction, obs_cells, obs_values):
    nx = lax.axis_size("dx")
    nz = lax.axis_size("dz")
    n_dom = nx * nz
    mx = lax.axis_index("dx")
    mz = lax.axis_index("dz")
    me = mx * nz + mz

    fore = forecast_of(state, depth, friction)

    eta = fore[0, 0].reshape(-1)
    seen = jnp.take(eta, obs_cells[0], axis=0)
    gap = seen - obs_values[0]
    partial_value = -jnp.sum(gap * gap) * (0.5 / obs_variance)
    if LOGLIK_MODE == "psum":
        slots = jnp.where(jnp.arange(n_dom) == me, partial_value, 0.0)
        by_source = lax.psum(slots, ("dx", "dz", "strip"))
    elif LOGLIK_MODE == "a2a":
        n_all = n_dom * lax.axis_size("strip")
        spread = jnp.broadcast_to(partial_value, (n_all, 1))
        every = lax.all_to_all(spread, ("dx", "dz", "strip"), 0, 0, tiled=True)
        by_source = jnp.sum(every.reshape(n_dom, -1), axis=1)
    else:
        slots = jnp.where(jnp.arange(n_dom) == me, partial_value, 0.0)
        by_source = butterfly_sum(slots, (("strip", lax.axis_size("strip")), ("dx", nx), ("dz", nz)))

    if STAGE1 == "gather":
        along_z = lax.all_gather(fore[0], "dz", axis=0, tiled=False)
    else:
        parts = [None] * nz
        parts[0] = fore[0]
        for d in range(1, nz):
            parts[d] = lax.ppermute(fore[0], "dz", [(i, (i + d) % nz) for i in range(nz)])
        order = jnp.stack(parts)
        along_z = jnp.take(order, (mz - jnp.arange(nz)) % nz, axis=0)
    dest = jnp.arange(nx) * nz + mz
    src = copies[dest]
    picks = jnp.stack([lax.dynamic_index_in_dim(along_z, src[k] % nz, axis=0, keepdims=False) for k in range(nx)])
    if STAGE2 == "a2a":
        moved = lax.all_to_all(picks, "dx", 0, 0, tiled=False)
    else:
        got = [None] * nx
        got[0] = lax.dynamic_index_in_dim(picks, mx, axis=0, keepdims=False)
        for d in range(1, nx):
            send = lax.dynamic_index_in_dim(picks, (mx + d) % nx, axis=0, keepdims=False)
            got[d] = lax.ppermute(send, "dx", [(i, (i + d) % nx) for i in range(nx)])
        moved = jnp.take(jnp.stack(got), (mx - jnp.arange(nx)) % nx, axis=0)
    mine_src = copies[me]
    member = lax.dynamic_index_in_dim(moved, mine_src // nz, axis=0, keepdims=True)

    loglik = by_source[copies]
    top = jnp.max(loglik)
    total = top + jnp.log(jnp.sum(jnp.exp(loglik - top)))
    mine = lax.dynamic_slice_in_dim(loglik - total, me, 1, 0)
    return (member, mine)


def solution(mesh):
    n_dom = mesh.shape["dom"]
    xs = sorted({d.coords[0] for d in mesh.devices[:, 0]})
    nx = len(xs)
    devices = mesh.devices.reshape(nx, n_dom // nx, mesh.shape["strip"])
    split = Mesh(devices, ("dx", "dz", "strip"))
    placed = (
        P(DOM, None, "strip", None),
        P(),
        P("strip", None),
        P("strip", None),
        P("strip", None),
        P("strip", None),
    )
    return jax.shard_map(
        local,
        mesh=split,
        in_specs=placed,
        out_specs=(P(DOM, None, "strip", None), P(DOM)),
        check_vma=False,
    )
```

```python
import functools

import jax
import jax.numpy as jnp
from jax import lax
from jax.sharding import Mesh
from jax.experimental import pallas as pl
from jax.experimental.pallas import tpu as pltpu
from jax.sharding import PartitionSpec as P

STEPS = 4


time_step = 0.25
coriolis = 0.3
diffusion = 0.2
obs_variance = 4.0

DOM = ("dx", "dz")
LOGLIK_MODE = "a2a"
STAGE1 = "gather"
STAGE2 = "a2a"


def diff_cols(a):
    return (jnp.roll(a, -1, axis=-1) - jnp.roll(a, 1, axis=-1)) * 0.5


def advance(padded, deep, drag, valid):
    eta, velo_u, velo_v, tracer = (padded[:, 0], padded[:, 1], padded[:, 2], padded[:, 3])
    flux_x = deep * velo_u
    flux_y = deep * velo_v
    eta_ext = eta[:, 1:-1] - time_step * (
        diff_cols(flux_x)[:, 1:-1] + (flux_y[:, 2:] - flux_y[:, :-2]) * 0.5
    )
    eta_ext = jnp.where(valid, eta_ext, 0.0)
    eta_new = eta_ext[:, 1:-1]
    inner_u = velo_u[:, 2:-2]
    inner_v = velo_v[:, 2:-2]
    inner_r = drag[2:-2]
    u_new = (
        inner_u
        - time_step * diff_cols(eta_new)
        - time_step * inner_r * inner_u
        + time_step * coriolis * inner_v
    )
    v_new = (
        inner_v
        - time_step * ((eta_ext[:, 2:] - eta_ext[:, :-2]) * 0.5)
        - time_step * inner_r * inner_v
        - time_step * coriolis * inner_u
    )
    inner_c = tracer[:, 2:-2]
    upper = tracer[:, 3:-1]
    lower = tracer[:, 1:-3]
    grad_y = (upper - lower) * 0.5
    laplace = (
        upper
        + lower
        + jnp.roll(inner_c, -1, axis=-1)
        + jnp.roll(inner_c, 1, axis=-1)
        - 4.0 * inner_c
    )
    c_new = (
        inner_c
        - time_step * (inner_u * diff_cols(inner_c) + inner_v * grad_y)
        + time_step * diffusion * laplace
    )
    return jnp.stack([eta_new, u_new, v_new, c_new], axis=1)


def halo_frame(cells, width):
    count = lax.axis_size("strip")
    ends = count - 1
    rows = cells.shape[1]
    head = cells[:, :width]
    tail = cells[:, rows - width:]
    above = lax.ppermute(tail, "strip", [(i, i + 1) for i in range(ends)])
    below = lax.ppermute(head, "strip", [(i + 1, i) for i in range(ends)])
    return jnp.concatenate([above, cells, below], axis=1)


def _steps_kernel(total_rows, base_ref, state_ref, deep_ref, drag_ref, above_ref, below_ref, out_ref):
    def frame(k, own):
        return jnp.concatenate([above_ref[k], own, below_ref[k]], axis=0)

    eta = frame(0, state_ref[0])
    velo_u = frame(1, state_ref[1])
    velo_v = frame(2, state_ref[2])
    tracer = frame(3, state_ref[3])
    deep = frame(4, deep_ref[...])
    drag = frame(5, drag_ref[...])
    rows, cols = eta.shape
    row = base_ref[0] + lax.broadcasted_iota(jnp.int32, (rows, cols), 0)
    inside = (row >= 0) & (row < total_rows)

    def east(a):
        return pltpu.roll(a, cols - 1, 1)

    def west(a):
        return pltpu.roll(a, 1, 1)

    def north(a):
        return pltpu.roll(a, rows - 1, 0)

    def south(a):
        return pltpu.roll(a, 1, 0)

    def dcols(a):
        return (east(a) - west(a)) * 0.5

    for _ in range(STEPS):
        flux_x = deep * velo_u
        flux_y = deep * velo_v
        eta_new = eta - time_step * (dcols(flux_x) + (north(flux_y) - south(flux_y)) * 0.5)
        eta_new = jnp.where(inside, eta_new, 0.0)
        u_new = (
            velo_u
            - time_step * dcols(eta_new)
            - time_step * drag * velo_u
            + time_step * coriolis * velo_v
        )
        v_new = (
            velo_v
            - time_step * ((north(eta_new) - south(eta_new)) * 0.5)
            - time_step * drag * velo_v
            - time_step * coriolis * velo_u
        )
        upper = north(tracer)
        lower = south(tracer)
        grad_y = (upper - lower) * 0.5
        laplace = upper + lower + east(tracer) + west(tracer) - 4.0 * tracer
        c_new = (
            tracer
            - time_step * (velo_u * dcols(tracer) + velo_v * grad_y)
            + time_step * diffusion * laplace
        )
        eta = eta_new
        velo_u = jnp.where(inside, u_new, 0.0)
        velo_v = jnp.where(inside, v_new, 0.0)
        tracer = jnp.where(inside, c_new, 0.0)
    margin = 2 * STEPS
    own = rows - 2 * margin
    out_ref[0, 0] = eta[margin : margin + own]
    out_ref[0, 1] = velo_u[margin : margin + own]
    out_ref[0, 2] = velo_v[margin : margin + own]
    out_ref[0, 3] = tracer[margin : margin + own]


def forecast_of(state, depth, friction):
    rows = state.shape[2]
    cols = state.shape[3]
    margin = 2 * STEPS
    count = lax.axis_size("strip")
    ends = count - 1
    packed = jnp.concatenate([state[0], depth[None], friction[None]], axis=0)
    above = lax.ppermute(packed[:, rows - margin:], "strip", [(i, i + 1) for i in range(ends)])
    below = lax.ppermute(packed[:, :margin], "strip", [(i + 1, i) for i in range(ends)])
    base = (lax.axis_index("strip") * rows - margin).astype(jnp.int32).reshape(1)
    vmem = pl.BlockSpec(memory_space=pltpu.VMEM)
    smem = pl.BlockSpec(memory_space=pltpu.SMEM)
    return pl.pallas_call(
        functools.partial(_steps_kernel, rows * count),
        out_shape=jax.ShapeDtypeStruct(state.shape, state.dtype),
        in_specs=[smem] + [vmem] * 5,
        out_specs=vmem,
    )(base, state[0], depth, friction, above, below)


def butterfly_sum(value, axes):
    for axis, size in axes:
        step = 1
        while step < size:
            pairs = [(i, i ^ step) for i in range(size)]
            value = value + lax.ppermute(value, axis, pairs)
            step *= 2
    return value


def local(state, copies, depth, friction, obs_cells, obs_values):
    nx = lax.axis_size("dx")
    nz = lax.axis_size("dz")
    n_dom = nx * nz
    mx = lax.axis_index("dx")
    mz = lax.axis_index("dz")
    me = mx * nz + mz

    fore = forecast_of(state, depth, friction)

    eta = fore[0, 0].reshape(-1)
    seen = jnp.take(eta, obs_cells[0], axis=0)
    gap = seen - obs_values[0]
    partial_value = -jnp.sum(gap * gap) * (0.5 / obs_variance)
    if LOGLIK_MODE == "psum":
        slots = jnp.where(jnp.arange(n_dom) == me, partial_value, 0.0)
        by_source = lax.psum(slots, ("dx", "dz", "strip"))
    elif LOGLIK_MODE == "a2a":
        n_all = n_dom * lax.axis_size("strip")
        spread = jnp.broadcast_to(partial_value, (n_all, 1))
        every = lax.all_to_all(spread, ("dx", "dz", "strip"), 0, 0, tiled=True)
        by_source = jnp.sum(every.reshape(n_dom, -1), axis=1)
    else:
        slots = jnp.where(jnp.arange(n_dom) == me, partial_value, 0.0)
        by_source = butterfly_sum(slots, (("strip", lax.axis_size("strip")), ("dx", nx), ("dz", nz)))

    if STAGE1 == "gather":
        along_z = lax.all_gather(fore[0], "dz", axis=0, tiled=False)
    else:
        parts = [None] * nz
        parts[0] = fore[0]
        for d in range(1, nz):
            parts[d] = lax.ppermute(fore[0], "dz", [(i, (i + d) % nz) for i in range(nz)])
        order = jnp.stack(parts)
        along_z = jnp.take(order, (mz - jnp.arange(nz)) % nz, axis=0)
    dest = jnp.arange(nx) * nz + mz
    src = copies[dest]
    picks = jnp.stack([lax.dynamic_index_in_dim(along_z, src[k] % nz, axis=0, keepdims=False) for k in range(nx)])
    if STAGE2 == "a2a":
        moved = lax.all_to_all(picks, "dx", 0, 0, tiled=False)
    else:
        got = [None] * nx
        got[0] = lax.dynamic_index_in_dim(picks, mx, axis=0, keepdims=False)
        for d in range(1, nx):
            send = lax.dynamic_index_in_dim(picks, (mx + d) % nx, axis=0, keepdims=False)
            got[d] = lax.ppermute(send, "dx", [(i, (i + d) % nx) for i in range(nx)])
        moved = jnp.take(jnp.stack(got), (mx - jnp.arange(nx)) % nx, axis=0)
    mine_src = copies[me]
    member = lax.dynamic_index_in_dim(moved, mine_src // nz, axis=0, keepdims=True)

    loglik = by_source[copies]
    top = jnp.max(loglik)
    total = top + jnp.log(jnp.sum(jnp.exp(loglik - top)))
    mine = lax.dynamic_slice_in_dim(loglik - total, me, 1, 0)
    return (member, mine)


def solution(mesh):
    n_dom = mesh.shape["dom"]
    xs = sorted({d.coords[0] for d in mesh.devices[:, 0]})
    nx = len(xs)
    devices = mesh.devices.reshape(nx, n_dom // nx, mesh.shape["strip"])
    split = Mesh(devices, ("dx", "dz", "strip"))
    placed = (
        P(DOM, None, "strip", None),
        P(),
        P("strip", None),
        P("strip", None),
        P("strip", None),
        P("strip", None),
    )
    return jax.shard_map(
        local,
        mesh=split,
        in_specs=placed,
        out_specs=(P(DOM, None, "strip", None), P(DOM)),
        check_vma=False,
    )
```

```python
import functools

import jax
import jax.numpy as jnp
from jax import lax
from jax.sharding import Mesh
from jax.experimental import pallas as pl
from jax.experimental.pallas import tpu as pltpu
from jax.sharding import PartitionSpec as P

STEPS = 4


time_step = 0.25
coriolis = 0.3
diffusion = 0.2
obs_variance = 4.0

DOM = ("dx", "dz")
LOGLIK_MODE = "a2a"
STAGE1 = "gather"
STAGE2 = "a2a"


def diff_cols(a):
    return (jnp.roll(a, -1, axis=-1) - jnp.roll(a, 1, axis=-1)) * 0.5


def advance(padded, deep, drag, valid):
    eta, velo_u, velo_v, tracer = (padded[:, 0], padded[:, 1], padded[:, 2], padded[:, 3])
    flux_x = deep * velo_u
    flux_y = deep * velo_v
    eta_ext = eta[:, 1:-1] - time_step * (
        diff_cols(flux_x)[:, 1:-1] + (flux_y[:, 2:] - flux_y[:, :-2]) * 0.5
    )
    eta_ext = jnp.where(valid, eta_ext, 0.0)
    eta_new = eta_ext[:, 1:-1]
    inner_u = velo_u[:, 2:-2]
    inner_v = velo_v[:, 2:-2]
    inner_r = drag[2:-2]
    u_new = (
        inner_u
        - time_step * diff_cols(eta_new)
        - time_step * inner_r * inner_u
        + time_step * coriolis * inner_v
    )
    v_new = (
        inner_v
        - time_step * ((eta_ext[:, 2:] - eta_ext[:, :-2]) * 0.5)
        - time_step * inner_r * inner_v
        - time_step * coriolis * inner_u
    )
    inner_c = tracer[:, 2:-2]
    upper = tracer[:, 3:-1]
    lower = tracer[:, 1:-3]
    grad_y = (upper - lower) * 0.5
    laplace = (
        upper
        + lower
        + jnp.roll(inner_c, -1, axis=-1)
        + jnp.roll(inner_c, 1, axis=-1)
        - 4.0 * inner_c
    )
    c_new = (
        inner_c
        - time_step * (inner_u * diff_cols(inner_c) + inner_v * grad_y)
        + time_step * diffusion * laplace
    )
    return jnp.stack([eta_new, u_new, v_new, c_new], axis=1)


def halo_frame(cells, width):
    count = lax.axis_size("strip")
    ends = count - 1
    rows = cells.shape[1]
    head = cells[:, :width]
    tail = cells[:, rows - width:]
    above = lax.ppermute(tail, "strip", [(i, i + 1) for i in range(ends)])
    below = lax.ppermute(head, "strip", [(i + 1, i) for i in range(ends)])
    return jnp.concatenate([above, cells, below], axis=1)


def _steps_kernel(total_rows, base_ref, state_ref, deep_ref, drag_ref, above_ref, below_ref, out_ref):
    def frame(k, own):
        return jnp.concatenate([above_ref[k], own, below_ref[k]], axis=0)

    eta = frame(0, state_ref[0])
    velo_u = frame(1, state_ref[1])
    velo_v = frame(2, state_ref[2])
    tracer = frame(3, state_ref[3])
    deep = frame(4, deep_ref[...])
    drag = frame(5, drag_ref[...])
    rows, cols = eta.shape
    row = base_ref[0] + lax.broadcasted_iota(jnp.int32, (rows, cols), 0)
    inside = (row >= 0) & (row < total_rows)

    def east(a):
        return pltpu.roll(a, cols - 1, 1)

    def west(a):
        return pltpu.roll(a, 1, 1)

    def north(a):
        return pltpu.roll(a, rows - 1, 0)

    def south(a):
        return pltpu.roll(a, 1, 0)

    def dcols(a):
        return (east(a) - west(a)) * 0.5

    for _ in range(STEPS):
        flux_x = deep * velo_u
        flux_y = deep * velo_v
        eta_new = eta - time_step * (dcols(flux_x) + (north(flux_y) - south(flux_y)) * 0.5)
        eta_new = jnp.where(inside, eta_new, 0.0)
        u_new = (
            velo_u
            - time_step * dcols(eta_new)
            - time_step * drag * velo_u
            + time_step * coriolis * velo_v
        )
        v_new = (
            velo_v
            - time_step * ((north(eta_new) - south(eta_new)) * 0.5)
            - time_step * drag * velo_v
            - time_step * coriolis * velo_u
        )
        upper = north(tracer)
        lower = south(tracer)
        grad_y = (upper - lower) * 0.5
        laplace = upper + lower + east(tracer) + west(tracer) - 4.0 * tracer
        c_new = (
            tracer
            - time_step * (velo_u * dcols(tracer) + velo_v * grad_y)
            + time_step * diffusion * laplace
        )
        eta = eta_new
        velo_u = jnp.where(inside, u_new, 0.0)
        velo_v = jnp.where(inside, v_new, 0.0)
        tracer = jnp.where(inside, c_new, 0.0)
    margin = 2 * STEPS
    own = rows - 2 * margin
    out_ref[0, 0] = eta[margin : margin + own]
    out_ref[0, 1] = velo_u[margin : margin + own]
    out_ref[0, 2] = velo_v[margin : margin + own]
    out_ref[0, 3] = tracer[margin : margin + own]


def forecast_of(state, depth, friction):
    rows = state.shape[2]
    cols = state.shape[3]
    margin = 2 * STEPS
    count = lax.axis_size("strip")
    ends = count - 1
    packed = jnp.concatenate([state[0], depth[None], friction[None]], axis=0)
    above = lax.ppermute(packed[:, rows - margin:], "strip", [(i, i + 1) for i in range(ends)])
    below = lax.ppermute(packed[:, :margin], "strip", [(i + 1, i) for i in range(ends)])
    base = (lax.axis_index("strip") * rows - margin).astype(jnp.int32).reshape(1)
    vmem = pl.BlockSpec(memory_space=pltpu.VMEM)
    smem = pl.BlockSpec(memory_space=pltpu.SMEM)
    return pl.pallas_call(
        functools.partial(_steps_kernel, rows * count),
        out_shape=jax.ShapeDtypeStruct(state.shape, state.dtype),
        in_specs=[smem] + [vmem] * 5,
        out_specs=vmem,
    )(base, state[0], depth, friction, above, below)


def butterfly_sum(value, axes):
    for axis, size in axes:
        step = 1
        while step < size:
            pairs = [(i, i ^ step) for i in range(size)]
            value = value + lax.ppermute(value, axis, pairs)
            step *= 2
    return value


def local(state, copies, depth, friction, obs_cells, obs_values):
    nx = lax.axis_size("dx")
    nz = lax.axis_size("dz")
    n_dom = nx * nz
    mx = lax.axis_index("dx")
    mz = lax.axis_index("dz")
    me = mx * nz + mz

    fore = forecast_of(state, depth, friction)

    eta = fore[0, 0].reshape(-1)
    seen = jnp.take(eta, obs_cells[0], axis=0)
    gap = seen - obs_values[0]
    partial_value = -jnp.sum(gap * gap) * (0.5 / obs_variance)
    if LOGLIK_MODE == "psum":
        slots = jnp.where(jnp.arange(n_dom) == me, partial_value, 0.0)
        by_source = lax.psum(slots, ("dx", "dz", "strip"))
    elif LOGLIK_MODE == "a2a":
        n_strip = lax.axis_size("strip")
        spread = jnp.broadcast_to(partial_value, (n_strip, 1))
        strips = lax.all_to_all(spread, "strip", 0, 0, tiled=True)
        mine_total = jnp.sum(strips)
        spread2 = jnp.broadcast_to(mine_total, (n_dom, 1))
        every = lax.all_to_all(spread2, ("dx", "dz"), 0, 0, tiled=True)
        by_source = every.reshape(n_dom)
    else:
        slots = jnp.where(jnp.arange(n_dom) == me, partial_value, 0.0)
        by_source = butterfly_sum(slots, (("strip", lax.axis_size("strip")), ("dx", nx), ("dz", nz)))

    if STAGE1 == "gather":
        along_z = lax.all_gather(fore[0], "dz", axis=0, tiled=False)
    else:
        parts = [None] * nz
        parts[0] = fore[0]
        for d in range(1, nz):
            parts[d] = lax.ppermute(fore[0], "dz", [(i, (i + d) % nz) for i in range(nz)])
        order = jnp.stack(parts)
        along_z = jnp.take(order, (mz - jnp.arange(nz)) % nz, axis=0)
    dest = jnp.arange(nx) * nz + mz
    src = copies[dest]
    picks = jnp.stack([lax.dynamic_index_in_dim(along_z, src[k] % nz, axis=0, keepdims=False) for k in range(nx)])
    if STAGE2 == "a2a":
        moved = lax.all_to_all(picks, "dx", 0, 0, tiled=False)
    else:
        got = [None] * nx
        got[0] = lax.dynamic_index_in_dim(picks, mx, axis=0, keepdims=False)
        for d in range(1, nx):
            send = lax.dynamic_index_in_dim(picks, (mx + d) % nx, axis=0, keepdims=False)
            got[d] = lax.ppermute(send, "dx", [(i, (i + d) % nx) for i in range(nx)])
        moved = jnp.take(jnp.stack(got), (mx - jnp.arange(nx)) % nx, axis=0)
    mine_src = copies[me]
    member = lax.dynamic_index_in_dim(moved, mine_src // nz, axis=0, keepdims=True)

    loglik = by_source[copies]
    top = jnp.max(loglik)
    total = top + jnp.log(jnp.sum(jnp.exp(loglik - top)))
    mine = lax.dynamic_slice_in_dim(loglik - total, me, 1, 0)
    return (member, mine)


def solution(mesh):
    n_dom = mesh.shape["dom"]
    xs = sorted({d.coords[0] for d in mesh.devices[:, 0]})
    nx = len(xs)
    devices = mesh.devices.reshape(nx, n_dom // nx, mesh.shape["strip"])
    split = Mesh(devices, ("dx", "dz", "strip"))
    placed = (
        P(DOM, None, "strip", None),
        P(),
        P("strip", None),
        P("strip", None),
        P("strip", None),
        P("strip", None),
    )
    return jax.shard_map(
        local,
        mesh=split,
        in_specs=placed,
        out_specs=(P(DOM, None, "strip", None), P(DOM)),
        check_vma=False,
    )
```
